1024 devices in a mesh: view: 4 (over y_hi, core), row: 32 (over x, y_lo), col: 8 (over z).
Axes of the slice: x: 8, y: 8 (y_hi: 2, y_lo: 4; y = y_hi * 4 + y_lo), z: 8, core: 2. Of those that a mesh axis runs over, the one named last changes fastest.
Arguments:
- estimate: float32 [256, 512, 128], P('col', 'row'), may hold values from 0.5 to 2
- views: bfloat16 [8, 256, 512, 128], P('view', 'col', 'row'), may hold values from 0.3 to 41.5, as said below
- kernel_xdir: float32 [8, 31], P('view'), may hold values from 0.2 to 1.2, as said below
- kernel_ydir: float32 [8, 31], P('view'), may hold values from 0.2 to 1.2, as said below
- kernel_axial: float32 [8, 121], P('view'), may hold values from 0.2 to 1.2, as said below
Outputs:
- restored: float32 [256, 512, 128], P('col', 'row')
The draws below stay inside these ranges and needn't reach their ends.
Inputs may be any that keep to these rules, and one draw needn't show every extreme that they name: `kernel_xdir`: every tap is positive. `kernel_ydir`: every tap is positive. `kernel_axial`: every tap is positive. `views`: every value is positive.
All inputs are finite; a program needn't handle non-finite values.
Results may differ from the reference program's by a relative error of at most 0.00035.
Values may be sent and summed in bfloat16 or wider, within the bound.
No kernel may reach another device: no remote copies, remote signals or barrier semaphores. Data moves between devices by JAX's collectives and lax.ppermute only.
A program may use at most 32 MiB of HBM per device.

```python
import math
import jax
import jax.numpy as jnp
from jax import lax

NX = 128
TAPS_LAT = 31
TAPS_AX = 121
ITERS = 2
NY = 512
NZ = 256
VIEWS = 8


def peaked_rows(key, taps, widths):
    offsets = jnp.arange(taps, dtype=jnp.float32) - (taps - 1) / 2.0
    profile = jnp.exp(-(offsets[None, :] * offsets[None, :]) / (2.0 * widths * widths))
    factor = jax.random.uniform(jax.random.fold_in(key, 5), (VIEWS, taps), jnp.float32, 0.8, 1.2)
    return factor * (0.3 + 0.7 * profile)


def spread_widths(key, low, high):
    widths = jnp.exp(jax.random.uniform(jax.random.fold_in(key, 3), (VIEWS, 1), jnp.float32, math.log(low), math.log(high)))
    return widths


def draw_kernel_xdir(key, part):
    own_key = jax.random.fold_in(key, 101)
    return peaked_rows(own_key, TAPS_LAT, spread_widths(own_key, 0.8, 2.5))


def draw_kernel_ydir(key, part):
    own_key = jax.random.fold_in(key, 202)
    return peaked_rows(own_key, TAPS_LAT, spread_widths(own_key, 0.8, 2.5))


def draw_kernel_axial(key, part):
    own_key = jax.random.fold_in(key, 303)
    return peaked_rows(own_key, TAPS_AX, spread_widths(own_key, 3.0, 12.0))


def draw_views(key, part):
    beads = jax.random.bernoulli(jax.random.fold_in(key, 11), 1.0 / 48.0, (NZ, NY, NX)).astype(jnp.float32)
    blocks_z = (NZ + 7) // 8
    blocks_y = (NY + 7) // 8
    bright = jnp.exp(jax.random.uniform(jax.random.fold_in(key, 12), (NZ, NY, NX), jnp.float32, math.log(10.0), math.log(40.0)))
    levels = jnp.exp(jax.random.uniform(jax.random.fold_in(key, 15), (blocks_z, blocks_y), jnp.float32, math.log(0.35), math.log(1.3)))
    spread_levels = jnp.repeat(jnp.repeat(levels, 8, axis=0), 8, axis=1)[:NZ, :NY]
    jitter = jax.random.uniform(jax.random.fold_in(key, 13), (VIEWS, NZ, NY, NX), jnp.float32, 0.86, 1.15)
    backdrop = spread_levels[None, :, :, None] * jitter
    visible = jax.random.uniform(jax.random.fold_in(key, 14), (VIEWS, NZ, NY, NX), jnp.float32, 0.7, 1.0)
    return (backdrop + visible * (beads * bright)[None]).astype(jnp.bfloat16)


def shard_levels(rng, shape, split, least, top_value):
    def one(dim, shards_of):
        draws = jax.random.uniform(jax.random.fold_in(jax.random.fold_in(rng, 6), dim), (shards_of,), jnp.float32, least / len(split), top_value / len(split))
        return jnp.repeat(jnp.exp(draws), shape[dim] // shards_of).reshape((-1,) + (1,) * (len(shape) - dim - 1))

    gain = one(*split[0])
    for cut in split[1:]:
        gain = gain * one(*cut)
    return gain


def setup_inputs(seed: int = 0) -> dict:
    splits = jax.random.split(jax.random.key(seed), 6)
    return {
        "estimate": jnp.clip(jnp.exp(math.log(2.0) - 1.3862944 * jax.random.uniform(splits[0], (NZ, NY, NX), jnp.float32) ** shard_levels(splits[0], (NZ, NY, NX), ((0, 8), (1, 32)), -0.2, 0.2)), 0.5, 2.0),
        "views": draw_views(jax.random.fold_in(splits[5], 71), 0),
        "kernel_xdir": draw_kernel_xdir(jax.random.fold_in(splits[5], 71), 0),
        "kernel_ydir": draw_kernel_ydir(jax.random.fold_in(splits[5], 71), 0),
        "kernel_axial": draw_kernel_axial(jax.random.fold_in(splits[5], 71), 0),
    }


def settle(field):
    return lax.optimization_barrier(field.astype(jnp.bfloat16)).astype(jnp.float32)


def toeplitz_band(kernel, height, breadth, offset):
    extent = height + breadth
    zeros_pad = jnp.zeros((extent,), kernel.dtype)
    padded = jnp.concatenate([zeros_pad, kernel, zeros_pad])
    leading = lax.slice_in_dim(padded, extent + offset, extent + offset + breadth)
    trailing = lax.slice_in_dim(padded, extent + offset - height, extent + offset)
    ribbon = jnp.concatenate([leading, trailing])
    tiled = jnp.tile(ribbon, height)[: height * (extent - 1)]
    return tiled.reshape(height, extent - 1)[:, :breadth]


def reference(estimate, views, kernel_xdir, kernel_ydir, kernel_axial):
    taps_xdir = settle(kernel_xdir / jnp.sum(kernel_xdir, axis=1, keepdims=True))
    taps_ydir = settle(kernel_ydir / jnp.sum(kernel_ydir, axis=1, keepdims=True))
    taps_axial = settle(kernel_axial / jnp.sum(kernel_axial, axis=1, keepdims=True))
    radius_lat = kernel_xdir.shape[1] // 2
    radius_ax = kernel_axial.shape[1] // 2
    high = lax.Precision.HIGHEST
    restored = estimate
    for iteration in range(ITERS):
        coarse = settle(restored)
        accumulated = jnp.zeros(restored.shape, jnp.float32)
        for member in range(VIEWS):
            band_x = toeplitz_band(taps_xdir[member], NX, NX, radius_lat)
            band_y = toeplitz_band(taps_ydir[member], NY, NY, radius_lat)
            band_z = toeplitz_band(taps_axial[member], NZ, NZ, radius_ax)
            smeared = settle(jnp.einsum("zyj,ij->zyi", coarse, band_x, precision=high))
            lateral = settle(jnp.einsum("ij,zjx->zix", band_y, smeared, precision=high))
            blurred = jnp.einsum("ij,jyx->iyx", band_z, lateral, precision=high)
            quotient = settle(views[member].astype(jnp.float32) / blurred)
            returned = settle(jnp.einsum("ij,iyx->jyx", band_z, quotient, precision=high))
            backward = settle(jnp.einsum("ij,zix->zjx", band_y, returned, precision=high))
            accumulated = accumulated + jnp.einsum("zyi,ij->zyj", backward, band_x, precision=high)
        restored = restored * accumulated / VIEWS
    return restored
```

```python
import jax
import jax.numpy as jnp
from jax import lax
from jax.sharding import PartitionSpec as P

ITERS = 2


def extended(shard, sides, width):
    for axis, dim in sides:
        count, length = (lax.axis_size(axis), shard.shape[dim])
        up = [(i, (i + 1) % count) for i in range(count - 1)]
        down = [(j, i) for i, j in up]
        last = lax.slice_in_dim(shard, length - width, length, axis=dim)
        initial = lax.slice_in_dim(shard, 0, width, axis=dim)
        before = lax.ppermute(last, axis, up)
        after = lax.ppermute(initial, axis, down)
        shard = jnp.concatenate([before, shard, after], axis=dim)
    return shard


def butterfly_sum(value, axis):
    count = lax.axis_size(axis)
    assert count & (count - 1) == 0
    stride = 1
    while stride < count:
        pairs = [(i, i ^ stride) for i in range(count)]
        value = value + lax.ppermute(value, axis, pairs)
        stride *= 2
    return value


def toeplitz_band(kernel, height, breadth, offset):
    extent = height + breadth
    zeros_pad = jnp.zeros((extent,), kernel.dtype)
    padded = jnp.concatenate([zeros_pad, kernel, zeros_pad])
    leading = lax.slice_in_dim(padded, extent + offset, extent + offset + breadth)
    trailing = lax.slice_in_dim(padded, extent + offset - height, extent + offset)
    ribbon = jnp.concatenate([leading, trailing])
    tiled = jnp.tile(ribbon, height)[: height * (extent - 1)]
    return tiled.reshape(height, extent - 1)[:, :breadth]


def normalized(kernel):
    return (kernel / jnp.sum(kernel, axis=1, keepdims=True)).astype(jnp.bfloat16)


def on_device(estimate, views, kernel_xdir, kernel_ydir, kernel_axial):
    planes_local, height, across = estimate.shape
    planes = planes_local * lax.axis_size("col")
    view_count = views.shape[0]
    total_views = view_count * lax.axis_size("view")
    radius_lat = kernel_xdir.shape[1] // 2
    radius_ax = kernel_axial.shape[1] // 2
    taps_xdir = normalized(kernel_xdir)
    taps_ydir = normalized(kernel_ydir)
    taps_axial = normalized(kernel_axial)
    framed_rows = height + 2 * radius_lat
    bands_x = jnp.stack(
        [
            toeplitz_band(taps_xdir[member], across, across, radius_lat)
            for member in range(view_count)
        ]
    )
    bands_y = jnp.stack(
        [toeplitz_band(taps_ydir[member], height, framed_rows, 0) for member in range(view_count)]
    )
    bands_yback = jnp.stack(
        [
            toeplitz_band(taps_ydir[member][::-1], height, framed_rows, 0)
            for member in range(view_count)
        ]
    )
    bands_z = jnp.stack(
        [
            toeplitz_band(taps_axial[member], planes, planes, radius_ax)
            for member in range(view_count)
        ]
    )

    def framed(field):
        return extended(field, (("row", 2),), radius_lat)

    def to_columns(field):
        return lax.all_to_all(field, "col", split_axis=3, concat_axis=1, tiled=True)

    view_columns = to_columns(views)
    column_shape = view_columns.shape
    column_width = column_shape[2] * column_shape[3]
    view_columns = view_columns.reshape(view_count, planes, column_width)

    def correct(coarse, opening, amount):
        chosen = slice(opening, opening + amount)
        matrix_x = bands_x[chosen]
        matrix_y = bands_y[chosen]
        matrix_yback = bands_yback[chosen]
        matrix_z = bands_z[chosen]
        smeared = jnp.einsum(
            "zyj,vij->vzyi", coarse, matrix_x, preferred_element_type=jnp.float32
        ).astype(jnp.bfloat16)
        lateral = jnp.einsum(
            "vij,vzjx->vzix", matrix_y, framed(smeared), preferred_element_type=jnp.float32
        ).astype(jnp.bfloat16)
        columns = to_columns(lateral)
        blurred = jnp.einsum(
            "vij,vjm->vim",
            matrix_z,
            columns.reshape(amount, planes, column_width),
            preferred_element_type=jnp.float32,
        )
        quotient = (view_columns[chosen] / blurred).astype(jnp.bfloat16)
        returned = jnp.einsum(
            "vij,vim->vjm", matrix_z, quotient, preferred_element_type=jnp.float32
        ).astype(jnp.bfloat16)
        slab_back = lax.all_to_all(
            returned.reshape(columns.shape), "col", split_axis=1, concat_axis=3, tiled=True
        )
        backward = jnp.einsum(
            "vij,vzjx->vzix", matrix_yback, framed(slab_back), preferred_element_type=jnp.float32
        ).astype(jnp.bfloat16)
        return jnp.einsum("vzyi,vij->zyj", backward, matrix_x, preferred_element_type=jnp.float32)

    restored = estimate
    for iteration in range(ITERS):
        coarse = restored.astype(jnp.bfloat16)
        accumulated = correct(coarse, 0, view_count)
        summed = butterfly_sum(accumulated, "view")
        restored = restored * summed / total_views
    return restored


def solution(mesh):
    placed = (
        P("col", "row", None),
        P("view", "col", "row", None),
        P("view", None),
        P("view", None),
        P("view", None),
    )
    return jax.shard_map(
        on_device, mesh=mesh, in_specs=placed, out_specs=P("col", "row", None), check_vma=False
    )
```

```python
import jax
import jax.numpy as jnp
from jax import lax
from jax.sharding import PartitionSpec as P

ITERS = 2


def extended(shard, sides, width):
    for axis, dim in sides:
        count, length = (lax.axis_size(axis), shard.shape[dim])
        up = [(i, (i + 1) % count) for i in range(count - 1)]
        down = [(j, i) for i, j in up]
        last = lax.slice_in_dim(shard, length - width, length, axis=dim)
        initial = lax.slice_in_dim(shard, 0, width, axis=dim)
        before = lax.ppermute(last, axis, up)
        after = lax.ppermute(initial, axis, down)
        shard = jnp.concatenate([before, shard, after], axis=dim)
    return shard


def butterfly_sum(value, axis):
    count = lax.axis_size(axis)
    assert count & (count - 1) == 0
    stride = 1
    while stride < count:
        pairs = [(i, i ^ stride) for i in range(count)]
        value = value + lax.ppermute(value, axis, pairs)
        stride *= 2
    return value


def toeplitz_band(kernel, height, breadth, offset):
    extent = height + breadth
    zeros_pad = jnp.zeros((extent,), kernel.dtype)
    padded = jnp.concatenate([zeros_pad, kernel, zeros_pad])
    leading = lax.slice_in_dim(padded, extent + offset, extent + offset + breadth)
    trailing = lax.slice_in_dim(padded, extent + offset - height, extent + offset)
    ribbon = jnp.concatenate([leading, trailing])
    tiled = jnp.tile(ribbon, height)[: height * (extent - 1)]
    return tiled.reshape(height, extent - 1)[:, :breadth]


def normalized(kernel):
    return (kernel / jnp.sum(kernel, axis=1, keepdims=True)).astype(jnp.bfloat16)


def on_device(estimate, views, kernel_xdir, kernel_ydir, kernel_axial):
    planes_local, height, across = estimate.shape
    planes = planes_local * lax.axis_size("col")
    view_count = views.shape[0]
    total_views = view_count * lax.axis_size("view")
    radius_lat = kernel_xdir.shape[1] // 2
    radius_ax = kernel_axial.shape[1] // 2
    taps_xdir = normalized(kernel_xdir)
    taps_ydir = normalized(kernel_ydir)
    taps_axial = normalized(kernel_axial)
    framed_rows = height + 2 * radius_lat
    bands_x = jnp.stack(
        [
            toeplitz_band(taps_xdir[member], across, across, radius_lat)
            for member in range(view_count)
        ]
    )
    bands_y = jnp.stack(
        [toeplitz_band(taps_ydir[member], height, framed_rows, 0) for member in range(view_count)]
    )
    bands_yback = jnp.stack(
        [
            toeplitz_band(taps_ydir[member][::-1], height, framed_rows, 0)
            for member in range(view_count)
        ]
    )
    bands_z = jnp.stack(
        [
            toeplitz_band(taps_axial[member], planes, planes, radius_ax)
            for member in range(view_count)
        ]
    )

    def framed(field):
        return extended(field, (("row", 2),), radius_lat)

    def framed_rows_of(field):
        return extended(field, (("row", 1),), radius_lat)

    def to_columns(field):
        return lax.all_to_all(field, "col", split_axis=3, concat_axis=1, tiled=True)

    view_columns = to_columns(views)
    column_shape = view_columns.shape
    column_width = column_shape[2] * column_shape[3]
    view_columns = view_columns.reshape(view_count, planes, column_width)

    def correct(coarse_framed, opening, amount):
        chosen = slice(opening, opening + amount)
        matrix_x = bands_x[chosen]
        matrix_y = bands_y[chosen]
        matrix_yback = bands_yback[chosen]
        matrix_z = bands_z[chosen]
        smeared = jnp.einsum(
            "zyj,vij->vzyi", coarse_framed, matrix_x, preferred_element_type=jnp.float32
        ).astype(jnp.bfloat16)
        lateral = jnp.einsum(
            "vij,vzjx->vzix", matrix_y, smeared, preferred_element_type=jnp.float32
        ).astype(jnp.bfloat16)
        columns = to_columns(lateral)
        blurred = jnp.einsum(
            "vij,vjm->vim",
            matrix_z,
            columns.reshape(amount, planes, column_width),
            preferred_element_type=jnp.float32,
        )
        quotient = (view_columns[chosen] / blurred).astype(jnp.bfloat16)
        returned = jnp.einsum(
            "vij,vim->vjm", matrix_z, quotient, preferred_element_type=jnp.float32
        ).astype(jnp.bfloat16)
        slab_back = lax.all_to_all(
            returned.reshape(columns.shape), "col", split_axis=1, concat_axis=3, tiled=True
        )
        backward = jnp.einsum(
            "vij,vzjx->vzix", matrix_yback, framed(slab_back), preferred_element_type=jnp.float32
        ).astype(jnp.bfloat16)
        return jnp.einsum("vzyi,vij->zyj", backward, matrix_x, preferred_element_type=jnp.float32)

    half = planes_local // 2
    core_bit = lax.axis_index("view") % 2
    view_size = lax.axis_size("view")
    to_core = [(i, i ^ 1) for i in range(view_size)]
    to_far = [(i, i ^ 2) for i in range(view_size)]

    def pick(field, which):
        return lax.dynamic_slice_in_dim(field, which * half, half, axis=0)

    def joined(mine, theirs):
        return jnp.where(
            core_bit == 0,
            jnp.concatenate([mine, theirs], axis=0),
            jnp.concatenate([theirs, mine], axis=0),
        )

    restored_mine = pick(estimate, core_bit)
    coarse = estimate.astype(jnp.bfloat16)
    for iteration in range(ITERS):
        if iteration:
            coarse_mine = restored_mine.astype(jnp.bfloat16)
            coarse = joined(coarse_mine, lax.ppermute(coarse_mine, "view", to_core))
        accumulated = correct(framed_rows_of(coarse), 0, view_count)
        paired = pick(accumulated, core_bit) + lax.ppermute(
            pick(accumulated, 1 - core_bit), "view", to_core
        )
        summed = paired + lax.ppermute(paired, "view", to_far)
        restored_mine = restored_mine * summed / total_views
    restored = joined(restored_mine, lax.ppermute(restored_mine, "view", to_core))
    return restored


def solution(mesh):
    placed = (
        P("col", "row", None),
        P("view", "col", "row", None),
        P("view", None),
        P("view", None),
        P("view", None),
    )
    return jax.shard_map(
        on_device, mesh=mesh, in_specs=placed, out_specs=P("col", "row", None), check_vma=False
    )
```

```python
import jax
import jax.numpy as jnp
from jax import lax
from jax.sharding import PartitionSpec as P

ITERS = 2


def extended(shard, sides, width):
    for axis, dim in sides:
        count, length = (lax.axis_size(axis), shard.shape[dim])
        up = [(i, (i + 1) % count) for i in range(count - 1)]
        down = [(j, i) for i, j in up]
        last = lax.slice_in_dim(shard, length - width, length, axis=dim)
        initial = lax.slice_in_dim(shard, 0, width, axis=dim)
        before = lax.ppermute(last, axis, up)
        after = lax.ppermute(initial, axis, down)
        shard = jnp.concatenate([before, shard, after], axis=dim)
    return shard


def butterfly_sum(value, axis):
    count = lax.axis_size(axis)
    assert count & (count - 1) == 0
    stride = 1
    while stride < count:
        pairs = [(i, i ^ stride) for i in range(count)]
        value = value + lax.ppermute(value, axis, pairs)
        stride *= 2
    return value


def toeplitz_band(kernel, height, breadth, offset):
    extent = height + breadth
    zeros_pad = jnp.zeros((extent,), kernel.dtype)
    padded = jnp.concatenate([zeros_pad, kernel, zeros_pad])
    leading = lax.slice_in_dim(padded, extent + offset, extent + offset + breadth)
    trailing = lax.slice_in_dim(padded, extent + offset - height, extent + offset)
    ribbon = jnp.concatenate([leading, trailing])
    tiled = jnp.tile(ribbon, height)[: height * (extent - 1)]
    return tiled.reshape(height, extent - 1)[:, :breadth]


def normalized(kernel):
    return (kernel / jnp.sum(kernel, axis=1, keepdims=True)).astype(jnp.bfloat16)


def on_device(estimate, views, kernel_xdir, kernel_ydir, kernel_axial):
    planes_local, height, across = estimate.shape
    planes = planes_local * lax.axis_size("col")
    view_count = views.shape[0]
    total_views = view_count * lax.axis_size("view")
    radius_lat = kernel_xdir.shape[1] // 2
    radius_ax = kernel_axial.shape[1] // 2
    taps_xdir = normalized(kernel_xdir)
    taps_ydir = normalized(kernel_ydir)
    taps_axial = normalized(kernel_axial)
    framed_rows = height + 2 * radius_lat
    bands_x = jnp.stack(
        [
            toeplitz_band(taps_xdir[member], across, across, radius_lat)
            for member in range(view_count)
        ]
    )
    bands_y = jnp.stack(
        [toeplitz_band(taps_ydir[member], height, framed_rows, 0) for member in range(view_count)]
    )
    bands_yback = jnp.stack(
        [
            toeplitz_band(taps_ydir[member][::-1], height, framed_rows, 0)
            for member in range(view_count)
        ]
    )
    bands_z = jnp.stack(
        [
            toeplitz_band(taps_axial[member], planes, planes, radius_ax)
            for member in range(view_count)
        ]
    )

    def framed(field):
        return extended(field, (("row", 2),), radius_lat)

    def framed_rows_of(field):
        return extended(field, (("row", 1),), radius_lat)

    blocks = lax.axis_size("col")
    pair = height // blocks
    column_width = pair * across

    def to_columns(field):
        amount = field.shape[0]
        chunks = field.reshape(amount, planes_local, blocks, pair, across)
        chunks = chunks.transpose(2, 0, 1, 3, 4).reshape(blocks, amount * planes_local, column_width)
        gathered = lax.all_to_all(chunks, "col", split_axis=0, concat_axis=0, tiled=True)
        return gathered.reshape(blocks, amount, planes_local, column_width)

    def to_slabs(columns):
        amount = columns.shape[0]
        chunks = columns.reshape(amount, blocks, planes_local, column_width).transpose(1, 0, 2, 3)
        chunks = chunks.reshape(blocks, amount * planes_local, column_width)
        spread = lax.all_to_all(chunks, "col", split_axis=0, concat_axis=0, tiled=True)
        spread = spread.reshape(blocks, amount, planes_local, pair, across)
        return spread.transpose(1, 2, 0, 3, 4).reshape(amount, planes_local, height, across)

    view_columns = (
        to_columns(views).transpose(1, 0, 2, 3).reshape(view_count, planes, column_width)
    )

    def correct(coarse_framed, opening, amount):
        chosen = slice(opening, opening + amount)
        matrix_x = bands_x[chosen]
        matrix_y = bands_y[chosen]
        matrix_yback = bands_yback[chosen]
        matrix_z = bands_z[chosen]
        smeared = jnp.einsum(
            "zyj,vij->vzyi", coarse_framed, matrix_x, preferred_element_type=jnp.float32
        ).astype(jnp.bfloat16)
        lateral = jnp.einsum(
            "vij,vzjx->vzix", matrix_y, smeared, preferred_element_type=jnp.float32
        ).astype(jnp.bfloat16)
        columns = to_columns(lateral)
        blurred = jnp.einsum(
            "visz,svzm->vim",
            matrix_z.reshape(amount, planes, blocks, planes_local),
            columns,
            preferred_element_type=jnp.float32,
        )
        quotient = (view_columns[chosen] / blurred).astype(jnp.bfloat16)
        returned = jnp.einsum(
            "vij,vim->vjm", matrix_z, quotient, preferred_element_type=jnp.float32
        ).astype(jnp.bfloat16)
        slab_back = to_slabs(returned)
        backward = jnp.einsum(
            "vij,vzjx->vzix", matrix_yback, framed(slab_back), preferred_element_type=jnp.float32
        ).astype(jnp.bfloat16)
        return jnp.einsum("vzyi,vij->zyj", backward, matrix_x, preferred_element_type=jnp.float32)

    half = planes_local // 2
    core_bit = lax.axis_index("view") % 2
    view_size = lax.axis_size("view")
    to_core = [(i, i ^ 1) for i in range(view_size)]
    to_far = [(i, i ^ 2) for i in range(view_size)]

    def pick(field, which):
        return lax.dynamic_slice_in_dim(field, which * half, half, axis=0)

    def joined(mine, theirs):
        return jnp.where(
            core_bit == 0,
            jnp.concatenate([mine, theirs], axis=0),
            jnp.concatenate([theirs, mine], axis=0),
        )

    restored_mine = pick(estimate, core_bit)
    coarse = estimate.astype(jnp.bfloat16)
    for iteration in range(ITERS):
        if iteration:
            coarse_mine = restored_mine.astype(jnp.bfloat16)
            coarse = joined(coarse_mine, lax.ppermute(coarse_mine, "view", to_core))
        accumulated = correct(framed_rows_of(coarse), 0, view_count)
        paired = pick(accumulated, core_bit) + lax.ppermute(
            pick(accumulated, 1 - core_bit), "view", to_core
        )
        summed = paired + lax.ppermute(paired, "view", to_far)
        restored_mine = restored_mine * summed / total_views
    restored = joined(restored_mine, lax.ppermute(restored_mine, "view", to_core))
    return restored


def solution(mesh):
    placed = (
        P("col", "row", None),
        P("view", "col", "row", None),
        P("view", None),
        P("view", None),
        P("view", None),
    )
    return jax.shard_map(
        on_device, mesh=mesh, in_specs=placed, out_specs=P("col", "row", None), check_vma=False
    )
```

```python
import jax
import jax.numpy as jnp
from jax import lax
from jax.sharding import PartitionSpec as P

ITERS = 2


def extended(shard, sides, width):
    for axis, dim in sides:
        count, length = (lax.axis_size(axis), shard.shape[dim])
        up = [(i, (i + 1) % count) for i in range(count - 1)]
        down = [(j, i) for i, j in up]
        last = lax.slice_in_dim(shard, length - width, length, axis=dim)
        initial = lax.slice_in_dim(shard, 0, width, axis=dim)
        before = lax.ppermute(last, axis, up)
        after = lax.ppermute(initial, axis, down)
        shard = jnp.concatenate([before, shard, after], axis=dim)
    return shard


def butterfly_sum(value, axis):
    count = lax.axis_size(axis)
    assert count & (count - 1) == 0
    stride = 1
    while stride < count:
        pairs = [(i, i ^ stride) for i in range(count)]
        value = value + lax.ppermute(value, axis, pairs)
        stride *= 2
    return value


def toeplitz_band(kernel, height, breadth, offset):
    extent = height + breadth
    zeros_pad = jnp.zeros((extent,), kernel.dtype)
    padded = jnp.concatenate([zeros_pad, kernel, zeros_pad])
    leading = lax.slice_in_dim(padded, extent + offset, extent + offset + breadth)
    trailing = lax.slice_in_dim(padded, extent + offset - height, extent + offset)
    ribbon = jnp.concatenate([leading, trailing])
    tiled = jnp.tile(ribbon, height)[: height * (extent - 1)]
    return tiled.reshape(height, extent - 1)[:, :breadth]


def normalized(kernel):
    return (kernel / jnp.sum(kernel, axis=1, keepdims=True)).astype(jnp.bfloat16)


def on_device(estimate, views, kernel_xdir, kernel_ydir, kernel_axial):
    planes_local, height, across = estimate.shape
    planes = planes_local * lax.axis_size("col")
    view_count = views.shape[0]
    total_views = view_count * lax.axis_size("view")
    radius_lat = kernel_xdir.shape[1] // 2
    radius_ax = kernel_axial.shape[1] // 2
    taps_xdir = normalized(kernel_xdir)
    taps_ydir = normalized(kernel_ydir)
    taps_axial = normalized(kernel_axial)
    framed_rows = height + 2 * radius_lat
    bands_x = jnp.stack(
        [
            toeplitz_band(taps_xdir[member], across, across, radius_lat)
            for member in range(view_count)
        ]
    )
    bands_y = jnp.stack(
        [toeplitz_band(taps_ydir[member], height, framed_rows, 0) for member in range(view_count)]
    )
    bands_yback = jnp.stack(
        [
            toeplitz_band(taps_ydir[member][::-1], height, framed_rows, 0)
            for member in range(view_count)
        ]
    )
    bands_z = jnp.stack(
        [
            toeplitz_band(taps_axial[member], planes, planes, radius_ax)
            for member in range(view_count)
        ]
    )

    def framed(field):
        return extended(field, (("row", 2),), radius_lat)

    def framed_rows_of(field):
        return extended(field, (("row", 1),), radius_lat)

    blocks = lax.axis_size("col")
    pair = height // blocks
    column_width = pair * across

    def to_columns(field):
        amount = field.shape[0]
        chunks = field.reshape(amount, planes_local, blocks, pair, across)
        chunks = chunks.transpose(2, 0, 1, 3, 4).reshape(blocks, amount * planes_local, column_width)
        gathered = lax.all_to_all(chunks, "col", split_axis=0, concat_axis=0, tiled=True)
        return gathered.reshape(blocks, amount, planes_local, column_width)

    def to_slabs(columns):
        amount = columns.shape[0]
        chunks = columns.reshape(amount, blocks, planes_local, column_width).transpose(1, 0, 2, 3)
        chunks = chunks.reshape(blocks, amount * planes_local, column_width)
        spread = lax.all_to_all(chunks, "col", split_axis=0, concat_axis=0, tiled=True)
        spread = spread.reshape(blocks, amount, planes_local, pair, across)
        return spread.transpose(1, 2, 0, 3, 4).reshape(amount, planes_local, height, across)

    def as_planes(columns):
        amount = columns.shape[1]
        return columns.transpose(1, 0, 2, 3).reshape(amount, planes, column_width)

    def correct(coarse_framed, opening, amount, view_columns):
        chosen = slice(opening, opening + amount)
        matrix_x = bands_x[chosen]
        matrix_y = bands_y[chosen]
        matrix_yback = bands_yback[chosen]
        matrix_z = bands_z[chosen]
        smeared = jnp.einsum(
            "zyj,vij->vzyi", coarse_framed, matrix_x, preferred_element_type=jnp.float32
        ).astype(jnp.bfloat16)
        lateral = jnp.einsum(
            "vij,vzjx->vzix", matrix_y, smeared, preferred_element_type=jnp.float32
        ).astype(jnp.bfloat16)
        if view_columns is None:
            both = to_columns(jnp.concatenate([lateral, views[chosen]], axis=0))
            columns, view_columns = both[:, :amount], as_planes(both[:, amount:])
        else:
            columns = to_columns(lateral)
        blurred = jnp.einsum(
            "visz,svzm->vim",
            matrix_z.reshape(amount, planes, blocks, planes_local),
            columns,
            preferred_element_type=jnp.float32,
        )
        quotient = (view_columns / blurred).astype(jnp.bfloat16)
        returned = jnp.einsum(
            "vij,vim->vjm", matrix_z, quotient, preferred_element_type=jnp.float32
        ).astype(jnp.bfloat16)
        slab_back = to_slabs(returned)
        backward = jnp.einsum(
            "vij,vzjx->vzix", matrix_yback, framed(slab_back), preferred_element_type=jnp.float32
        ).astype(jnp.bfloat16)
        corrected = jnp.einsum(
            "vzyi,vij->zyj", backward, matrix_x, preferred_element_type=jnp.float32
        )
        return corrected, view_columns

    half = planes_local // 2
    core_bit = lax.axis_index("view") % 2
    view_size = lax.axis_size("view")
    to_core = [(i, i ^ 1) for i in range(view_size)]
    to_far = [(i, i ^ 2) for i in range(view_size)]

    def pick(field, which):
        return lax.dynamic_slice_in_dim(field, which * half, half, axis=0)

    def joined(mine, theirs):
        return jnp.where(
            core_bit == 0,
            jnp.concatenate([mine, theirs], axis=0),
            jnp.concatenate([theirs, mine], axis=0),
        )

    restored_mine = pick(estimate, core_bit)
    coarse = estimate.astype(jnp.bfloat16)
    view_columns = None
    for iteration in range(ITERS):
        if iteration:
            coarse_mine = restored_mine.astype(jnp.bfloat16)
            coarse = joined(coarse_mine, lax.ppermute(coarse_mine, "view", to_core))
        accumulated, view_columns = correct(framed_rows_of(coarse), 0, view_count, view_columns)
        paired = pick(accumulated, core_bit) + lax.ppermute(
            pick(accumulated, 1 - core_bit), "view", to_core
        )
        summed = paired + lax.ppermute(paired, "view", to_far)
        restored_mine = restored_mine * summed / total_views
    restored = joined(restored_mine, lax.ppermute(restored_mine, "view", to_core))
    return restored


def solution(mesh):
    placed = (
        P("col", "row", None),
        P("view", "col", "row", None),
        P("view", None),
        P("view", None),
        P("view", None),
    )
    return jax.shard_map(
        on_device, mesh=mesh, in_specs=placed, out_specs=P("col", "row", None), check_vma=False
    )
```

```python
import jax
import jax.numpy as jnp
from jax import lax
from jax.sharding import PartitionSpec as P

ITERS = 2


def extended(shard, sides, width):
    for axis, dim in sides:
        count, length = (lax.axis_size(axis), shard.shape[dim])
        up = [(i, (i + 1) % count) for i in range(count - 1)]
        down = [(j, i) for i, j in up]
        last = lax.slice_in_dim(shard, length - width, length, axis=dim)
        initial = lax.slice_in_dim(shard, 0, width, axis=dim)
        before = lax.ppermute(last, axis, up)
        after = lax.ppermute(initial, axis, down)
        shard = jnp.concatenate([before, shard, after], axis=dim)
    return shard


def toeplitz_band(kernel, height, breadth, offset):
    extent = height + breadth
    zeros_pad = jnp.zeros((extent,), kernel.dtype)
    padded = jnp.concatenate([zeros_pad, kernel, zeros_pad])
    leading = lax.slice_in_dim(padded, extent + offset, extent + offset + breadth)
    trailing = lax.slice_in_dim(padded, extent + offset - height, extent + offset)
    ribbon = jnp.concatenate([leading, trailing])
    tiled = jnp.tile(ribbon, height)[: height * (extent - 1)]
    return tiled.reshape(height, extent - 1)[:, :breadth]


def normalized(kernel):
    return (kernel / jnp.sum(kernel, axis=1, keepdims=True)).astype(jnp.bfloat16)


def on_device(estimate, views, kernel_xdir, kernel_ydir, kernel_axial):
    planes_local, height, across = estimate.shape
    blocks = lax.axis_size("col")
    planes = planes_local * blocks
    view_size = lax.axis_size("view")
    view_count = views.shape[0]
    total_views = view_count * view_size
    radius_lat = kernel_xdir.shape[1] // 2
    radius_ax = kernel_axial.shape[1] // 2
    framed_rows = height + 2 * radius_lat
    half = planes_local // 2
    pair = height // blocks
    column_width = pair * across
    core_bit = lax.axis_index("view") % 2
    to_core = [(i, i ^ 1) for i in range(view_size)]
    to_far = [(i, i ^ 2) for i in range(view_size)]
    group = 2 * blocks
    groups = [list(range(g * group, (g + 1) * group)) for g in range(view_size // 2)]

    def joined(mine, theirs):
        return jnp.where(
            core_bit == 0,
            jnp.concatenate([mine, theirs], axis=0),
            jnp.concatenate([theirs, mine], axis=0),
        )

    def chip_taps(kernel):
        return normalized(joined(kernel, lax.ppermute(kernel, "view", to_core)))

    chip_x = chip_taps(kernel_xdir)
    chip_y = chip_taps(kernel_ydir)
    taps_axial = normalized(kernel_axial)
    chip_count = chip_x.shape[0]
    bands_x = jnp.stack(
        [toeplitz_band(chip_x[member], across, across, radius_lat) for member in range(chip_count)]
    )
    bands_y = jnp.stack(
        [toeplitz_band(chip_y[member], height, framed_rows, 0) for member in range(chip_count)]
    )
    bands_yback = jnp.stack(
        [
            toeplitz_band(chip_y[member][::-1], height, framed_rows, 0)
            for member in range(chip_count)
        ]
    )
    bands_z = jnp.stack(
        [
            toeplitz_band(taps_axial[member], planes, planes, radius_ax)
            for member in range(view_count)
        ]
    )
    bands_z = bands_z.reshape(view_count, planes, blocks, 2, half)

    def framed(field):
        return extended(field, (("row", 2),), radius_lat)

    def chip_exchange(chunks):
        return lax.all_to_all(
            chunks, ("view", "col"), 0, 0, axis_index_groups=groups, tiled=True
        )

    def to_columns(field):
        chunks = field.reshape(2, view_count, half, blocks, pair, across)
        chunks = chunks.transpose(0, 3, 1, 2, 4, 5).reshape(group, view_count * half, column_width)
        gathered = chip_exchange(chunks)
        return gathered.reshape(2, blocks, view_count, half, column_width)

    def to_slabs(columns):
        chunks = columns.reshape(view_count, blocks, 2, half, column_width)
        chunks = chunks.transpose(2, 1, 0, 3, 4).reshape(group, view_count * half, column_width)
        spread = chip_exchange(chunks)
        spread = spread.reshape(2, blocks, view_count, half, pair, across)
        spread = spread.transpose(0, 2, 3, 1, 4, 5)
        return spread.reshape(chip_count, half, height, across)

    own = lax.all_to_all(
        views.reshape(view_count, planes_local, blocks, column_width).transpose(2, 0, 1, 3),
        "col",
        0,
        0,
        tiled=True,
    )
    view_columns = own.transpose(1, 0, 2, 3).reshape(view_count, planes, column_width)

    def correct(coarse_framed):
        smeared = jnp.einsum(
            "zyj,vij->vzyi", coarse_framed, bands_x, preferred_element_type=jnp.float32
        ).astype(jnp.bfloat16)
        lateral = jnp.einsum(
            "vij,vzjx->vzix", bands_y, smeared, preferred_element_type=jnp.float32
        ).astype(jnp.bfloat16)
        columns = to_columns(lateral)
        blurred = jnp.einsum(
            "vicbz,bcvzm->vim", bands_z, columns, preferred_element_type=jnp.float32
        )
        quotient = (view_columns / blurred).astype(jnp.bfloat16)
        returned = jnp.einsum(
            "vicbz,vim->vcbzm", bands_z, quotient, preferred_element_type=jnp.float32
        ).astype(jnp.bfloat16)
        backward = jnp.einsum(
            "vij,vzjx->vzix", bands_yback, framed(to_slabs(returned)),
            preferred_element_type=jnp.float32,
        ).astype(jnp.bfloat16)
        return jnp.einsum("vzyi,vij->zyj", backward, bands_x, preferred_element_type=jnp.float32)

    restored_mine = lax.dynamic_slice_in_dim(estimate, core_bit * half, half, axis=0)
    for iteration in range(ITERS):
        coarse_mine = restored_mine.astype(jnp.bfloat16)
        accumulated = correct(extended(coarse_mine, (("row", 1),), radius_lat))
        summed = accumulated + lax.ppermute(accumulated, "view", to_far)
        restored_mine = restored_mine * summed / total_views
    return joined(restored_mine, lax.ppermute(restored_mine, "view", to_core))


def solution(mesh):
    placed = (
        P("col", "row", None),
        P("view", "col", "row", None),
        P("view", None),
        P("view", None),
        P("view", None),
    )
    return jax.shard_map(
        on_device, mesh=mesh, in_specs=placed, out_specs=P("col", "row", None), check_vma=False
    )
```

```python
import jax
import jax.numpy as jnp
from jax import lax
from jax.sharding import PartitionSpec as P

ITERS = 2


def extended(shard, sides, width):
    for axis, dim in sides:
        count, length = (lax.axis_size(axis), shard.shape[dim])
        up = [(i, (i + 1) % count) for i in range(count - 1)]
        down = [(j, i) for i, j in up]
        last = lax.slice_in_dim(shard, length - width, length, axis=dim)
        initial = lax.slice_in_dim(shard, 0, width, axis=dim)
        before = lax.ppermute(last, axis, up)
        after = lax.ppermute(initial, axis, down)
        shard = jnp.concatenate([before, shard, after], axis=dim)
    return shard


def toeplitz_band(kernel, height, breadth, offset):
    extent = height + breadth
    zeros_pad = jnp.zeros((extent,), kernel.dtype)
    padded = jnp.concatenate([zeros_pad, kernel, zeros_pad])
    leading = lax.slice_in_dim(padded, extent + offset, extent + offset + breadth)
    trailing = lax.slice_in_dim(padded, extent + offset - height, extent + offset)
    ribbon = jnp.concatenate([leading, trailing])
    tiled = jnp.tile(ribbon, height)[: height * (extent - 1)]
    return tiled.reshape(height, extent - 1)[:, :breadth]


def normalized(kernel):
    return (kernel / jnp.sum(kernel, axis=1, keepdims=True)).astype(jnp.bfloat16)


def on_device(estimate, views, kernel_xdir, kernel_ydir, kernel_axial):
    planes_local, height, across = estimate.shape
    blocks = lax.axis_size("col")
    planes = planes_local * blocks
    view_size = lax.axis_size("view")
    view_count = views.shape[0]
    total_views = view_count * view_size
    radius_lat = kernel_xdir.shape[1] // 2
    radius_ax = kernel_axial.shape[1] // 2
    framed_rows = height + 2 * radius_lat
    half = planes_local // 2
    core_bit = lax.axis_index("view") % 2
    to_core = [(i, i ^ 1) for i in range(view_size)]
    to_far = [(i, i ^ 2) for i in range(view_size)]
    group = 2 * blocks
    groups = [list(range(g * group, (g + 1) * group)) for g in range(view_size // 2)]

    def joined(mine, theirs):
        return jnp.where(
            core_bit == 0,
            jnp.concatenate([mine, theirs], axis=0),
            jnp.concatenate([theirs, mine], axis=0),
        )

    def chip_taps(kernel):
        return normalized(joined(kernel, lax.ppermute(kernel, "view", to_core)))

    chip_x = chip_taps(kernel_xdir)
    chip_y = chip_taps(kernel_ydir)
    chip_z = chip_taps(kernel_axial)
    chip_count = chip_x.shape[0]
    bands_x = jnp.stack(
        [toeplitz_band(chip_x[member], across, across, radius_lat) for member in range(chip_count)]
    )
    bands_y = jnp.stack(
        [toeplitz_band(chip_y[member], height, framed_rows, 0) for member in range(chip_count)]
    )
    bands_yback = jnp.stack(
        [
            toeplitz_band(chip_y[member][::-1], height, framed_rows, 0)
            for member in range(chip_count)
        ]
    )
    bands_z = jnp.stack(
        [
            toeplitz_band(chip_z[member], planes, planes, radius_ax)
            for member in range(chip_count)
        ]
    )
    bands_z = bands_z.reshape(chip_count, planes, blocks, 2, half)

    def framed(field):
        return extended(field, (("row", 2),), radius_lat)

    def chip_exchange(chunks):
        return lax.all_to_all(
            chunks, ("view", "col"), 0, 0, axis_index_groups=groups, tiled=True
        )

    def by_row(field):
        lead, depth = field.shape[0], field.shape[1]
        chunks = field.reshape(lead, depth, blocks, 2, across).transpose(3, 2, 0, 1, 4)
        return chunks.reshape(group, lead * depth, across)

    def to_columns(lateral, own_views):
        chunks = by_row(lateral)
        width = chunks.shape[1]
        if own_views is not None:
            chunks = jnp.concatenate([chunks, by_row(own_views)], axis=1)
        gathered = chip_exchange(chunks)
        columns = gathered[:, :width].reshape(2, blocks, chip_count, half, across)
        if own_views is None:
            return columns, None
        placed = gathered[:, width:].reshape(2, blocks, view_count, planes_local, across)
        placed = placed.transpose(0, 2, 1, 3, 4).reshape(chip_count, planes, across)
        return columns, placed

    def to_slabs(returned):
        spread = chip_exchange(returned.reshape(group, chip_count * half, across))
        spread = spread.reshape(2, blocks, chip_count, half, across).transpose(2, 3, 1, 0, 4)
        return spread.reshape(chip_count, half, height, across)

    def correct(coarse_framed, view_columns):
        smeared = jnp.einsum(
            "zyj,vij->vzyi", coarse_framed, bands_x, preferred_element_type=jnp.float32
        ).astype(jnp.bfloat16)
        lateral = jnp.einsum(
            "vij,vzjx->vzix", bands_y, smeared, preferred_element_type=jnp.float32
        ).astype(jnp.bfloat16)
        if view_columns is None:
            columns, view_columns = to_columns(lateral, views)
        else:
            columns, _ = to_columns(lateral, None)
        blurred = jnp.einsum(
            "vicbz,bcvzm->vim", bands_z, columns, preferred_element_type=jnp.float32
        )
        quotient = (view_columns / blurred).astype(jnp.bfloat16)
        returned = jnp.einsum(
            "vicbz,vim->bcvzm", bands_z, quotient, preferred_element_type=jnp.float32
        ).astype(jnp.bfloat16)
        backward = jnp.einsum(
            "vij,vzjx->vzix", bands_yback, framed(to_slabs(returned)),
            preferred_element_type=jnp.float32,
        ).astype(jnp.bfloat16)
        corrected = jnp.einsum(
            "vzyi,vij->zyj", backward, bands_x, preferred_element_type=jnp.float32
        )
        return corrected, view_columns

    restored_mine = lax.dynamic_slice_in_dim(estimate, core_bit * half, half, axis=0)
    view_columns = None
    for iteration in range(ITERS):
        coarse_mine = restored_mine.astype(jnp.bfloat16)
        accumulated, view_columns = correct(
            extended(coarse_mine, (("row", 1),), radius_lat), view_columns
        )
        summed = accumulated + lax.ppermute(accumulated, "view", to_far)
        restored_mine = restored_mine * summed / total_views
    return joined(restored_mine, lax.ppermute(restored_mine, "view", to_core))


def solution(mesh):
    placed = (
        P("col", "row", None),
        P("view", "col", "row", None),
        P("view", None),
        P("view", None),
        P("view", None),
    )
    return jax.shard_map(
        on_device, mesh=mesh, in_specs=placed, out_specs=P("col", "row", None), check_vma=False
    )
```

```python
import jax
import jax.numpy as jnp
from jax import lax
from jax.sharding import PartitionSpec as P

ITERS = 2


def extended(shard, sides, width):
    for axis, dim in sides:
        count, length = (lax.axis_size(axis), shard.shape[dim])
        up = [(i, (i + 1) % count) for i in range(count - 1)]
        down = [(j, i) for i, j in up]
        last = lax.slice_in_dim(shard, length - width, length, axis=dim)
        initial = lax.slice_in_dim(shard, 0, width, axis=dim)
        before = lax.ppermute(last, axis, up)
        after = lax.ppermute(initial, axis, down)
        shard = jnp.concatenate([before, shard, after], axis=dim)
    return shard


def toeplitz_band(kernel, height, breadth, offset):
    extent = height + breadth
    zeros_pad = jnp.zeros((extent,), kernel.dtype)
    padded = jnp.concatenate([zeros_pad, kernel, zeros_pad])
    leading = lax.slice_in_dim(padded, extent + offset, extent + offset + breadth)
    trailing = lax.slice_in_dim(padded, extent + offset - height, extent + offset)
    ribbon = jnp.concatenate([leading, trailing])
    tiled = jnp.tile(ribbon, height)[: height * (extent - 1)]
    return tiled.reshape(height, extent - 1)[:, :breadth]


def normalized(kernel):
    return (kernel / jnp.sum(kernel, axis=1, keepdims=True)).astype(jnp.bfloat16)


def on_device(estimate, views, kernel_xdir, kernel_ydir, kernel_axial):
    planes_local, height, across = estimate.shape
    blocks = lax.axis_size("col")
    planes = planes_local * blocks
    view_size = lax.axis_size("view")
    view_count = views.shape[0]
    total_views = view_count * view_size
    radius_lat = kernel_xdir.shape[1] // 2
    radius_ax = kernel_axial.shape[1] // 2
    framed_rows = height + 2 * radius_lat
    half = planes_local // 2
    core_bit = lax.axis_index("view") % 2
    to_core = [(i, i ^ 1) for i in range(view_size)]
    to_far = [(i, i ^ 2) for i in range(view_size)]
    group = 2 * blocks
    groups = [list(range(g * group, (g + 1) * group)) for g in range(view_size // 2)]

    def joined(mine, theirs):
        return jnp.where(
            core_bit == 0,
            jnp.concatenate([mine, theirs], axis=0),
            jnp.concatenate([theirs, mine], axis=0),
        )

    own_taps = jnp.concatenate([kernel_xdir, kernel_ydir, kernel_axial], axis=1)
    taps = joined(own_taps, lax.ppermute(own_taps, "view", to_core))
    lateral_taps = kernel_xdir.shape[1]
    chip_x = normalized(taps[:, :lateral_taps])
    chip_y = normalized(taps[:, lateral_taps : 2 * lateral_taps])
    chip_z = normalized(taps[:, 2 * lateral_taps :])
    chip_count = chip_x.shape[0]
    bands_x = jnp.stack(
        [toeplitz_band(chip_x[member], across, across, radius_lat) for member in range(chip_count)]
    )
    bands_y = jnp.stack(
        [toeplitz_band(chip_y[member], height, framed_rows, 0) for member in range(chip_count)]
    )
    bands_yback = jnp.stack(
        [
            toeplitz_band(chip_y[member][::-1], height, framed_rows, 0)
            for member in range(chip_count)
        ]
    )
    bands_z = jnp.stack(
        [
            toeplitz_band(chip_z[member], planes, planes, radius_ax)
            for member in range(chip_count)
        ]
    )
    bands_z = bands_z.reshape(chip_count, planes, blocks, 2, half)

    def framed(field):
        return extended(field, (("row", 2),), radius_lat)

    def chip_exchange(chunks):
        return lax.all_to_all(
            chunks, ("view", "col"), 0, 0, axis_index_groups=groups, tiled=True
        )

    def by_row(field):
        lead, depth = field.shape[0], field.shape[1]
        chunks = field.reshape(lead, depth, blocks, 2, across).transpose(3, 2, 0, 1, 4)
        return chunks.reshape(group, lead * depth, across)

    def to_columns(lateral, own_views):
        chunks = by_row(lateral)
        width = chunks.shape[1]
        if own_views is not None:
            chunks = jnp.concatenate([chunks, by_row(own_views)], axis=1)
        gathered = chip_exchange(chunks)
        columns = gathered[:, :width].reshape(2, blocks, chip_count, half, across)
        if own_views is None:
            return columns, None
        placed = gathered[:, width:].reshape(2, blocks, view_count, planes_local, across)
        placed = placed.transpose(0, 2, 1, 3, 4).reshape(chip_count, planes, across)
        return columns, placed

    def to_slabs(returned):
        spread = chip_exchange(returned.reshape(group, chip_count * half, across))
        spread = spread.reshape(2, blocks, chip_count, half, across).transpose(2, 3, 1, 0, 4)
        return spread.reshape(chip_count, half, height, across)

    def correct(coarse_framed, view_columns):
        smeared = jnp.einsum(
            "zyj,vij->vzyi", coarse_framed, bands_x, preferred_element_type=jnp.float32
        ).astype(jnp.bfloat16)
        lateral = jnp.einsum(
            "vij,vzjx->vzix", bands_y, smeared, preferred_element_type=jnp.float32
        ).astype(jnp.bfloat16)
        if view_columns is None:
            columns, view_columns = to_columns(lateral, views)
        else:
            columns, _ = to_columns(lateral, None)
        blurred = jnp.einsum(
            "vicbz,bcvzm->vim", bands_z, columns, preferred_element_type=jnp.float32
        )
        quotient = (view_columns / blurred).astype(jnp.bfloat16)
        returned = jnp.einsum(
            "vicbz,vim->bcvzm", bands_z, quotient, preferred_element_type=jnp.float32
        ).astype(jnp.bfloat16)
        backward = jnp.einsum(
            "vij,vzjx->vzix", bands_yback, framed(to_slabs(returned)),
            preferred_element_type=jnp.float32,
        ).astype(jnp.bfloat16)
        corrected = jnp.einsum(
            "vzyi,vij->zyj", backward, bands_x, preferred_element_type=jnp.float32
        )
        return corrected, view_columns

    restored_mine = lax.dynamic_slice_in_dim(estimate, core_bit * half, half, axis=0)
    view_columns = None
    for iteration in range(ITERS):
        coarse_mine = restored_mine.astype(jnp.bfloat16)
        accumulated, view_columns = correct(
            extended(coarse_mine, (("row", 1),), radius_lat), view_columns
        )
        summed = accumulated + lax.ppermute(accumulated, "view", to_far)
        restored_mine = restored_mine * summed / total_views
    return joined(restored_mine, lax.ppermute(restored_mine, "view", to_core))


def solution(mesh):
    placed = (
        P("col", "row", None),
        P("view", "col", "row", None),
        P("view", None),
        P("view", None),
        P("view", None),
    )
    return jax.shard_map(
        on_device, mesh=mesh, in_specs=placed, out_specs=P("col", "row", None), check_vma=False
    )
```

```python
import jax
import jax.numpy as jnp
from jax import lax
from jax.sharding import PartitionSpec as P

ITERS = 2


def extended(shard, sides, width):
    for axis, dim in sides:
        count, length = (lax.axis_size(axis), shard.shape[dim])
        up = [(i, (i + 1) % count) for i in range(count - 1)]
        down = [(j, i) for i, j in up]
        before = lax.slice_in_dim(lax.ppermute(shard, axis, up), length - width, length, axis=dim)
        after = lax.slice_in_dim(lax.ppermute(shard, axis, down), 0, width, axis=dim)
        shard = jnp.concatenate([before, shard, after], axis=dim)
    return shard


def toeplitz_band(kernel, height, breadth, offset):
    extent = height + breadth
    zeros_pad = jnp.zeros((extent,), kernel.dtype)
    padded = jnp.concatenate([zeros_pad, kernel, zeros_pad])
    leading = lax.slice_in_dim(padded, extent + offset, extent + offset + breadth)
    trailing = lax.slice_in_dim(padded, extent + offset - height, extent + offset)
    ribbon = jnp.concatenate([leading, trailing])
    tiled = jnp.tile(ribbon, height)[: height * (extent - 1)]
    return tiled.reshape(height, extent - 1)[:, :breadth]


def normalized(kernel):
    return (kernel / jnp.sum(kernel, axis=1, keepdims=True)).astype(jnp.bfloat16)


def on_device(estimate, views, kernel_xdir, kernel_ydir, kernel_axial):
    planes_local, height, across = estimate.shape
    blocks = lax.axis_size("col")
    planes = planes_local * blocks
    view_size = lax.axis_size("view")
    view_count = views.shape[0]
    total_views = view_count * view_size
    radius_lat = kernel_xdir.shape[1] // 2
    radius_ax = kernel_axial.shape[1] // 2
    framed_rows = height + 2 * radius_lat
    half = planes_local // 2
    core_bit = lax.axis_index("view") % 2
    to_core = [(i, i ^ 1) for i in range(view_size)]
    to_far = [(i, i ^ 2) for i in range(view_size)]
    group = 2 * blocks
    groups = [list(range(g * group, (g + 1) * group)) for g in range(view_size // 2)]

    def joined(mine, theirs):
        return jnp.where(
            core_bit == 0,
            jnp.concatenate([mine, theirs], axis=0),
            jnp.concatenate([theirs, mine], axis=0),
        )

    own_taps = jnp.concatenate([kernel_xdir, kernel_ydir, kernel_axial], axis=1)
    taps = joined(own_taps, lax.ppermute(own_taps, "view", to_core))
    lateral_taps = kernel_xdir.shape[1]
    chip_x = normalized(taps[:, :lateral_taps])
    chip_y = normalized(taps[:, lateral_taps : 2 * lateral_taps])
    chip_z = normalized(taps[:, 2 * lateral_taps :])
    chip_count = chip_x.shape[0]
    bands_x = jnp.stack(
        [toeplitz_band(chip_x[member], across, across, radius_lat) for member in range(chip_count)]
    )
    bands_y = jnp.stack(
        [toeplitz_band(chip_y[member], height, framed_rows, 0) for member in range(chip_count)]
    )
    bands_yback = jnp.stack(
        [
            toeplitz_band(chip_y[member][::-1], height, framed_rows, 0)
            for member in range(chip_count)
        ]
    )
    bands_z = jnp.stack(
        [
            toeplitz_band(chip_z[member], planes, planes, radius_ax)
            for member in range(chip_count)
        ]
    )
    bands_z = bands_z.reshape(chip_count, planes, blocks, 2, half)

    def framed(field):
        return extended(field, (("row", 2),), radius_lat)

    def chip_exchange(chunks):
        return lax.all_to_all(
            chunks, ("view", "col"), 0, 0, axis_index_groups=groups, tiled=True
        )

    def by_row(field):
        lead, depth = field.shape[0], field.shape[1]
        chunks = field.reshape(lead, depth, blocks, 2, across).transpose(3, 2, 0, 1, 4)
        return chunks.reshape(group, lead * depth, across)

    def to_columns(lateral, own_views):
        chunks = by_row(lateral)
        width = chunks.shape[1]
        if own_views is not None:
            chunks = jnp.concatenate([chunks, by_row(own_views)], axis=1)
        gathered = chip_exchange(chunks)
        columns = gathered[:, :width].reshape(2, blocks, chip_count, half, across)
        if own_views is None:
            return columns, None
        placed = gathered[:, width:].reshape(2, blocks, view_count, planes_local, across)
        placed = placed.transpose(0, 2, 1, 3, 4).reshape(chip_count, planes, across)
        return columns, placed

    def to_slabs(returned):
        spread = chip_exchange(returned.reshape(group, chip_count * half, across))
        spread = spread.reshape(2, blocks, chip_count, half, across).transpose(2, 3, 1, 0, 4)
        return spread.reshape(chip_count, half, height, across)

    def correct(coarse_framed, view_columns):
        smeared = jnp.einsum(
            "zyj,vij->vzyi", coarse_framed, bands_x, preferred_element_type=jnp.float32
        ).astype(jnp.bfloat16)
        lateral = jnp.einsum(
            "vij,vzjx->vzix", bands_y, smeared, preferred_element_type=jnp.float32
        ).astype(jnp.bfloat16)
        if view_columns is None:
            columns, view_columns = to_columns(lateral, views)
        else:
            columns, _ = to_columns(lateral, None)
        blurred = jnp.einsum(
            "vicbz,bcvzm->vim", bands_z, columns, preferred_element_type=jnp.float32
        )
        quotient = (view_columns / blurred).astype(jnp.bfloat16)
        returned = jnp.einsum(
            "vicbz,vim->bcvzm", bands_z, quotient, preferred_element_type=jnp.float32
        ).astype(jnp.bfloat16)
        backward = jnp.einsum(
            "vij,vzjx->vzix", bands_yback, framed(to_slabs(returned)),
            preferred_element_type=jnp.float32,
        ).astype(jnp.bfloat16)
        corrected = jnp.einsum(
            "vzyi,vij->zyj", backward, bands_x, preferred_element_type=jnp.float32
        )
        return corrected, view_columns

    restored_mine = lax.dynamic_slice_in_dim(estimate, core_bit * half, half, axis=0)
    view_columns = None
    for iteration in range(ITERS):
        coarse_mine = restored_mine.astype(jnp.bfloat16)
        accumulated, view_columns = correct(
            extended(coarse_mine, (("row", 1),), radius_lat), view_columns
        )
        summed = accumulated + lax.ppermute(accumulated, "view", to_far)
        restored_mine = restored_mine * summed / total_views
    return joined(restored_mine, lax.ppermute(restored_mine, "view", to_core))


def solution(mesh):
    placed = (
        P("col", "row", None),
        P("view", "col", "row", None),
        P("view", None),
        P("view", None),
        P("view", None),
    )
    return jax.shard_map(
        on_device, mesh=mesh, in_specs=placed, out_specs=P("col", "row", None), check_vma=False
    )
```

```python
import jax
import jax.numpy as jnp
from jax import lax
from jax.sharding import PartitionSpec as P

ITERS = 2


def extended(shard, sides, width):
    for axis, dim in sides:
        count, length = (lax.axis_size(axis), shard.shape[dim])
        up = [(i, (i + 1) % count) for i in range(count - 1)]
        down = [(j, i) for i, j in up]
        last = lax.slice_in_dim(shard, length - width, length, axis=dim)
        initial = lax.slice_in_dim(shard, 0, width, axis=dim)
        before = lax.ppermute(last, axis, up)
        after = lax.ppermute(initial, axis, down)
        shard = jnp.concatenate([before, shard, after], axis=dim)
    return shard


def toeplitz_band(kernel, height, breadth, offset):
    extent = height + breadth
    zeros_pad = jnp.zeros((extent,), kernel.dtype)
    padded = jnp.concatenate([zeros_pad, kernel, zeros_pad])
    leading = lax.slice_in_dim(padded, extent + offset, extent + offset + breadth)
    trailing = lax.slice_in_dim(padded, extent + offset - height, extent + offset)
    ribbon = jnp.concatenate([leading, trailing])
    tiled = jnp.tile(ribbon, height)[: height * (extent - 1)]
    return tiled.reshape(height, extent - 1)[:, :breadth]


def normalized(kernel):
    return (kernel / jnp.sum(kernel, axis=1, keepdims=True)).astype(jnp.bfloat16)


def on_device(estimate, views, kernel_xdir, kernel_ydir, kernel_axial):
    planes_local, height, across = estimate.shape
    blocks = lax.axis_size("col")
    planes = planes_local * blocks
    view_size = lax.axis_size("view")
    view_count = views.shape[0]
    total_views = view_count * view_size
    radius_lat = kernel_xdir.shape[1] // 2
    radius_ax = kernel_axial.shape[1] // 2
    framed_rows = height + 2 * radius_lat
    half = planes_local // 2
    core_bit = lax.axis_index("view") % 2
    to_core = [(i, i ^ 1) for i in range(view_size)]
    to_far = [(i, i ^ 2) for i in range(view_size)]
    group = 2 * blocks
    groups = [list(range(g * group, (g + 1) * group)) for g in range(view_size // 2)]

    def joined(mine, theirs):
        return jnp.where(
            core_bit == 0,
            jnp.concatenate([mine, theirs], axis=0),
            jnp.concatenate([theirs, mine], axis=0),
        )

    own_taps = jnp.concatenate([kernel_xdir, kernel_ydir, kernel_axial], axis=1)
    taps = joined(own_taps, lax.ppermute(own_taps, "view", to_core))
    lateral_taps = kernel_xdir.shape[1]
    chip_x = normalized(taps[:, :lateral_taps])
    chip_y = normalized(taps[:, lateral_taps : 2 * lateral_taps])
    chip_z = normalized(taps[:, 2 * lateral_taps :])
    chip_count = chip_x.shape[0]
    def banded(taps, height_, breadth, offset):
        return jax.vmap(lambda row: toeplitz_band(row, height_, breadth, offset))(taps)

    bands_x = banded(chip_x, across, across, radius_lat)
    bands_y = banded(chip_y, height, framed_rows, 0)
    bands_yback = banded(chip_y[:, ::-1], height, framed_rows, 0)
    bands_z = banded(chip_z, planes, planes, radius_ax)
    bands_z = bands_z.reshape(chip_count, planes, blocks, 2, half)

    def framed(field):
        return extended(field, (("row", 2),), radius_lat)

    def chip_exchange(chunks):
        return lax.all_to_all(
            chunks, ("view", "col"), 0, 0, axis_index_groups=groups, tiled=True
        )

    def by_row(field):
        lead, depth = field.shape[0], field.shape[1]
        chunks = field.reshape(lead, depth, blocks, 2, across).transpose(3, 2, 0, 1, 4)
        return chunks.reshape(group, lead * depth, across)

    def to_columns(lateral, own_views):
        chunks = by_row(lateral)
        width = chunks.shape[1]
        if own_views is not None:
            chunks = jnp.concatenate([chunks, by_row(own_views)], axis=1)
        gathered = chip_exchange(chunks)
        columns = gathered[:, :width].reshape(2, blocks, chip_count, half, across)
        if own_views is None:
            return columns, None
        placed = gathered[:, width:].reshape(2, blocks, view_count, planes_local, across)
        placed = placed.transpose(0, 2, 1, 3, 4).reshape(chip_count, planes, across)
        return columns, placed

    def to_slabs(returned):
        spread = chip_exchange(returned.reshape(group, chip_count * half, across))
        spread = spread.reshape(2, blocks, chip_count, half, across).transpose(2, 3, 1, 0, 4)
        return spread.reshape(chip_count, half, height, across)

    def correct(coarse_framed, view_columns):
        smeared = jnp.einsum(
            "zyj,vij->vzyi", coarse_framed, bands_x, preferred_element_type=jnp.float32
        ).astype(jnp.bfloat16)
        lateral = jnp.einsum(
            "vij,vzjx->vzix", bands_y, smeared, preferred_element_type=jnp.float32
        ).astype(jnp.bfloat16)
        if view_columns is None:
            columns, view_columns = to_columns(lateral, views)
        else:
            columns, _ = to_columns(lateral, None)
        blurred = jnp.einsum(
            "vicbz,bcvzm->vim", bands_z, columns, preferred_element_type=jnp.float32
        )
        quotient = (view_columns / blurred).astype(jnp.bfloat16)
        returned = jnp.einsum(
            "vicbz,vim->bcvzm", bands_z, quotient, preferred_element_type=jnp.float32
        ).astype(jnp.bfloat16)
        backward = jnp.einsum(
            "vij,vzjx->vzix", bands_yback, framed(to_slabs(returned)),
            preferred_element_type=jnp.float32,
        ).astype(jnp.bfloat16)
        corrected = jnp.einsum(
            "vzyi,vij->zyj", backward, bands_x, preferred_element_type=jnp.float32
        )
        return corrected, view_columns

    restored_mine = lax.dynamic_slice_in_dim(estimate, core_bit * half, half, axis=0)
    view_columns = None
    for iteration in range(ITERS):
        coarse_mine = restored_mine.astype(jnp.bfloat16)
        accumulated, view_columns = correct(
            extended(coarse_mine, (("row", 1),), radius_lat), view_columns
        )
        summed = accumulated + lax.ppermute(accumulated, "view", to_far)
        restored_mine = restored_mine * summed / total_views
    return joined(restored_mine, lax.ppermute(restored_mine, "view", to_core))


def solution(mesh):
    placed = (
        P("col", "row", None),
        P("view", "col", "row", None),
        P("view", None),
        P("view", None),
        P("view", None),
    )
    return jax.shard_map(
        on_device, mesh=mesh, in_specs=placed, out_specs=P("col", "row", None), check_vma=False
    )
```

```python
import jax
import jax.numpy as jnp
from jax import lax
from jax.sharding import PartitionSpec as P

ITERS = 2


def extended(shard, sides, width):
    for axis, dim in sides:
        count, length = (lax.axis_size(axis), shard.shape[dim])
        up = [(i, (i + 1) % count) for i in range(count - 1)]
        down = [(j, i) for i, j in up]
        before = lax.slice_in_dim(lax.ppermute(shard, axis, up), length - width, length, axis=dim)
        after = lax.slice_in_dim(lax.ppermute(shard, axis, down), 0, width, axis=dim)
        shard = jnp.concatenate([before, shard, after], axis=dim)
    return shard


def toeplitz_band(kernel, height, breadth, offset):
    extent = height + breadth
    zeros_pad = jnp.zeros((extent,), kernel.dtype)
    padded = jnp.concatenate([zeros_pad, kernel, zeros_pad])
    leading = lax.slice_in_dim(padded, extent + offset, extent + offset + breadth)
    trailing = lax.slice_in_dim(padded, extent + offset - height, extent + offset)
    ribbon = jnp.concatenate([leading, trailing])
    tiled = jnp.tile(ribbon, height)[: height * (extent - 1)]
    return tiled.reshape(height, extent - 1)[:, :breadth]


def normalized(kernel):
    return (kernel / jnp.sum(kernel, axis=1, keepdims=True)).astype(jnp.bfloat16)


def on_device(estimate, views, kernel_xdir, kernel_ydir, kernel_axial):
    planes_local, height, across = estimate.shape
    blocks = lax.axis_size("col")
    planes = planes_local * blocks
    view_size = lax.axis_size("view")
    view_count = views.shape[0]
    total_views = view_count * view_size
    radius_lat = kernel_xdir.shape[1] // 2
    radius_ax = kernel_axial.shape[1] // 2
    framed_rows = height + 2 * radius_lat
    half = planes_local // 2
    core_bit = lax.axis_index("view") % 2
    to_core = [(i, i ^ 1) for i in range(view_size)]
    to_far = [(i, i ^ 2) for i in range(view_size)]
    group = 2 * blocks
    groups = [list(range(g * group, (g + 1) * group)) for g in range(view_size // 2)]

    def joined(mine, theirs):
        return jnp.where(
            core_bit == 0,
            jnp.concatenate([mine, theirs], axis=0),
            jnp.concatenate([theirs, mine], axis=0),
        )

    own_taps = jnp.concatenate([kernel_xdir, kernel_ydir, kernel_axial], axis=1)
    taps = joined(own_taps, lax.ppermute(own_taps, "view", to_core))
    lateral_taps = kernel_xdir.shape[1]
    chip_x = normalized(taps[:, :lateral_taps])
    chip_y = normalized(taps[:, lateral_taps : 2 * lateral_taps])
    chip_z = normalized(taps[:, 2 * lateral_taps :])
    chip_count = chip_x.shape[0]
    def banded(taps, height_, breadth, offset):
        return jax.vmap(lambda row: toeplitz_band(row, height_, breadth, offset))(taps)

    bands_x = banded(chip_x, across, across, radius_lat)
    bands_y = banded(chip_y, height, framed_rows, 0)
    bands_yback = banded(chip_y[:, ::-1], height, framed_rows, 0)
    bands_z = banded(chip_z, planes, planes, radius_ax)
    bands_z = bands_z.reshape(chip_count, planes, blocks, 2, half)

    def framed(field):
        return extended(field, (("row", 2),), radius_lat)

    def chip_exchange(chunks):
        return lax.all_to_all(
            chunks, ("view", "col"), 0, 0, axis_index_groups=groups, tiled=True
        )

    def by_row(field):
        lead, depth = field.shape[0], field.shape[1]
        chunks = field.reshape(lead, depth, blocks, 2, across).transpose(3, 2, 0, 1, 4)
        return chunks.reshape(group, lead * depth, across)

    def to_columns(lateral, own_views):
        chunks = by_row(lateral)
        width = chunks.shape[1]
        if own_views is not None:
            chunks = jnp.concatenate([chunks, by_row(own_views)], axis=1)
        gathered = chip_exchange(chunks)
        columns = gathered[:, :width].reshape(2, blocks, chip_count, half, across)
        if own_views is None:
            return columns, None
        placed = gathered[:, width:].reshape(2, blocks, view_count, planes_local, across)
        placed = placed.transpose(0, 2, 1, 3, 4).reshape(chip_count, planes, across)
        return columns, placed

    def to_slabs(returned):
        spread = chip_exchange(returned.reshape(group, chip_count * half, across))
        spread = spread.reshape(2, blocks, chip_count, half, across).transpose(2, 3, 1, 0, 4)
        return spread.reshape(chip_count, half, height, across)

    def correct(coarse_framed, view_columns):
        smeared = jnp.einsum(
            "zyj,vij->vzyi", coarse_framed, bands_x, preferred_element_type=jnp.float32
        ).astype(jnp.bfloat16)
        lateral = jnp.einsum(
            "vij,vzjx->vzix", bands_y, smeared, preferred_element_type=jnp.float32
        ).astype(jnp.bfloat16)
        if view_columns is None:
            columns, view_columns = to_columns(lateral, views)
        else:
            columns, _ = to_columns(lateral, None)
        blurred = jnp.einsum(
            "vicbz,bcvzm->vim", bands_z, columns, preferred_element_type=jnp.float32
        )
        quotient = (view_columns / blurred).astype(jnp.bfloat16)
        returned = jnp.einsum(
            "vicbz,vim->bcvzm", bands_z, quotient, preferred_element_type=jnp.float32
        ).astype(jnp.bfloat16)
        backward = jnp.einsum(
            "vij,vzjx->vzix", bands_yback, framed(to_slabs(returned)),
            preferred_element_type=jnp.float32,
        ).astype(jnp.bfloat16)
        corrected = jnp.einsum(
            "vzyi,vij->zyj", backward, bands_x, preferred_element_type=jnp.float32
        )
        return corrected, view_columns

    restored_mine = lax.dynamic_slice_in_dim(estimate, core_bit * half, half, axis=0)
    view_columns = None
    for iteration in range(ITERS):
        coarse_mine = restored_mine.astype(jnp.bfloat16)
        accumulated, view_columns = correct(
            extended(coarse_mine, (("row", 1),), radius_lat), view_columns
        )
        summed = accumulated + lax.ppermute(accumulated, "view", to_far)
        restored_mine = restored_mine * summed / total_views
    return joined(restored_mine, lax.ppermute(restored_mine, "view", to_core))


def solution(mesh):
    placed = (
        P("col", "row", None),
        P("view", "col", "row", None),
        P("view", None),
        P("view", None),
        P("view", None),
    )
    return jax.shard_map(
        on_device, mesh=mesh, in_specs=placed, out_specs=P("col", "row", None), check_vma=False
    )
```
